256 devices in a mesh: dp: 16 (over y, x), ctx: 16 (over z, core).
Axes of the slice: x: 4, y: 4, z: 8, core: 2. Of those that a mesh axis runs over, the one named last changes fastest.
Arguments:
- query_heads: bfloat16 [65536, 16, 128], P(('dp', 'ctx')), parts along dimension 0, may hold values from -64 to 64
- key_heads: bfloat16 [65536, 8, 128], P(('dp', 'ctx')), parts along dimension 0, may hold values from -64 to 64
- value_heads: bfloat16 [65536, 8, 128], P(('dp', 'ctx')), parts along dimension 0, may hold values from -6 to 6
- grad_out: bfloat16 [65536, 16, 128], P(('dp', 'ctx')), parts along dimension 0, may hold values from -6 to 6
- doc_ids: int32 [65536], P('dp'), parts along dimension 0, may hold values from 0 to 4, as said below
Outputs:
- attended: bfloat16 [65536, 16, 128], P(('dp', 'ctx')), parts along dimension 0
- grad_query: bfloat16 [65536, 16, 128], P(('dp', 'ctx')), parts along dimension 0
- grad_key: bfloat16 [65536, 8, 128], P(('dp', 'ctx')), parts along dimension 0
- grad_value: bfloat16 [65536, 8, 128], P(('dp', 'ctx')), parts along dimension 0
The draws below stay inside these ranges and needn't reach their ends.
There are 16 independent parts, one for each index of `dp`. The reference program is written for one: setup_inputs(seed, part) draws one part's arguments, and reference() takes and returns one part's arrays. A program takes and returns all parts, laid end to end along the dimension named above; each array names one. Nothing has to cross between parts.
Inputs may be any that keep to these rules, and one draw needn't show every extreme that they name: doc_ids starts at 0 and never falls; within each aligned block of 1024 tokens it rises by one exactly once, never at the block's first token.
All inputs are finite; a program needn't handle non-finite values.
Results may differ from the reference program's by a relative error of at most 0.012.
Values may be sent and summed in bfloat16 or wider, within the bound.
No kernel may reach another device: no remote copies, remote signals or barrier semaphores. Data moves between devices by JAX's collectives and lax.ppermute only.
A program may use at most 64 MiB of HBM per device.

```python
import jax
import jax.numpy as jnp
from jax import lax

WINDOW = 1024
HQ = 16
KVH = 8
HD = 128
TOK_DEV = 256
SEQ = 4096


def draw_query_heads(key, part):
    background = jnp.clip(jax.random.normal(jax.random.fold_in(key, 1), (SEQ, HQ, HD), jnp.float32), -4.0, 4.0)
    return jnp.clip(background, -64.0, 64.0).astype(jnp.bfloat16)


def draw_key_heads(key, part):
    background = jnp.clip(jax.random.normal(jax.random.fold_in(key, 2), (SEQ, KVH, HD), jnp.float32), -4.0, 4.0)
    return jnp.clip(background, -64.0, 64.0).astype(jnp.bfloat16)


def draw_doc_ids(key, part):
    positions = jnp.arange(SEQ)
    block_count = SEQ // WINDOW
    offsets = jax.random.randint(jax.random.fold_in(key, 3), (block_count,), 1, WINDOW)
    offsets = jnp.where(offsets % TOK_DEV == TOK_DEV // 2, offsets + 1, offsets)
    block_of = positions // WINDOW
    chosen = jnp.sum(jnp.where(block_of[:, None] == jnp.arange(block_count)[None, :], offsets[None, :], 0), axis=1)
    boundary = positions % WINDOW == chosen
    return jnp.cumsum(boundary.astype(jnp.int32)).astype(jnp.int32)


def block_levels(rng, dims, split, smallest, high):
    level = 1.0
    for position, blocks in split:
        steps = jax.random.uniform(jax.random.fold_in(jax.random.fold_in(rng, 6), position), (blocks,), jnp.float32, smallest / len(split), high / len(split))
        level = level * jnp.repeat(jnp.exp(steps), dims[position] // blocks).reshape((-1,) + (1,) * (len(dims) - 1 - position))
    return level


def centred(key, extent, width, most, split=(), kind=jnp.bfloat16):
    gain = block_levels(key, extent, split, -0.22, 0.18) if split else 1.0
    result = jax.random.normal(key, extent, jnp.float32) * width * gain
    return jnp.minimum(jnp.maximum(result, -most), most).astype(kind)


def setup_inputs(seed: int = 0, part: int = 0) -> dict:
    key_of = jax.random.split(jax.random.key(seed), 6)
    part_keys = jax.random.split(jax.random.fold_in(key_of[5], part), 6)
    query_heads = draw_query_heads(jax.random.fold_in(jax.random.fold_in(key_of[5], part), 71), part)
    key_heads = draw_key_heads(jax.random.fold_in(jax.random.fold_in(key_of[5], part), 71), part)
    value_heads = centred(part_keys[2], (SEQ, KVH, HD), 1.0, 6.0, ((0, 16),))
    grad_out = centred(part_keys[3], (SEQ, HQ, HD), 1.0, 6.0, ((0, 16),))
    doc_ids = draw_doc_ids(jax.random.fold_in(jax.random.fold_in(key_of[5], part), 71), part)
    return {"query_heads": query_heads, "key_heads": key_heads, "value_heads": value_heads, "grad_out": grad_out, "doc_ids": doc_ids}


QUERY_SCALE = 168.0 ** -0.5


def block_grads(q_blk, k_win, v_win, g_blk, q_docs, k_docs):
    row_count = q_blk.shape[0]
    col_count = k_win.shape[0]
    groups = k_win.shape[1]
    q_index = jnp.arange(row_count)[:, None]
    k_index = jnp.arange(col_count)[None, :]
    allowed = (q_docs[:, None] == k_docs[None, :]) & (k_index > q_index) & (k_index <= q_index + WINDOW)
    q_four = q_blk.astype(jnp.float32).reshape(row_count, groups, 2, -1)
    g_four = g_blk.astype(jnp.float32).reshape(row_count, groups, 2, -1)
    k_full = k_win.astype(jnp.float32)
    v_full = v_win.astype(jnp.float32)
    scores = QUERY_SCALE * jnp.einsum('rgad,cgd->garc', q_four, k_full)
    masked = jnp.where(allowed, scores, -jnp.inf)
    row_max = jnp.max(masked, axis=-1, keepdims=True)
    unnorm = jnp.exp(masked - row_max)
    weights = unnorm / jnp.sum(unnorm, axis=-1, keepdims=True)
    weights_b = weights.astype(jnp.bfloat16)
    wide_b = weights_b.astype(jnp.float32)
    attended = jnp.einsum('garc,cgd->rgad', wide_b, v_full).astype(jnp.bfloat16)
    row_dot = jnp.sum(g_four * attended.astype(jnp.float32), axis=-1)
    dprob = jnp.einsum('rgad,cgd->garc', g_four, v_full)
    dscore = (weights * (dprob - jnp.transpose(row_dot, (1, 2, 0))[..., None])).astype(jnp.bfloat16)
    dscore_f = dscore.astype(jnp.float32)
    grad_q = (QUERY_SCALE * jnp.einsum('garc,cgd->rgad', dscore_f, k_full)).astype(jnp.bfloat16)
    grad_k = (QUERY_SCALE * jnp.einsum('garc,rgad->cgd', dscore_f, q_four)).astype(jnp.bfloat16)
    grad_v = jnp.einsum('garc,rgad->cgd', wide_b, g_four).astype(jnp.bfloat16)
    return attended.reshape(q_blk.shape), grad_q.reshape(q_blk.shape), grad_k, grad_v


def reference(query_heads, key_heads, value_heads, grad_out, doc_ids):
    pieces = query_heads.shape[0] // TOK_DEV
    pad_keys = jnp.concatenate([jnp.zeros((WINDOW, KVH, HD), key_heads.dtype), key_heads], 0)
    pad_values = jnp.concatenate([jnp.zeros((WINDOW, KVH, HD), value_heads.dtype), value_heads], 0)
    pad_docs = jnp.concatenate([jnp.full((WINDOW,), -1, jnp.int32), doc_ids.astype(jnp.int32)], 0)

    def one_block(block_index):
        first_row = (block_index * TOK_DEV).astype(jnp.int32)
        q_blk = lax.dynamic_slice_in_dim(query_heads, first_row, TOK_DEV, 0)
        g_blk = lax.dynamic_slice_in_dim(grad_out, first_row, TOK_DEV, 0)
        q_docs = lax.dynamic_slice_in_dim(doc_ids.astype(jnp.int32), first_row, TOK_DEV, 0)
        k_win = lax.dynamic_slice_in_dim(pad_keys, first_row, WINDOW + TOK_DEV, 0)
        v_win = lax.dynamic_slice_in_dim(pad_values, first_row, WINDOW + TOK_DEV, 0)
        k_docs = lax.dynamic_slice_in_dim(pad_docs, first_row, WINDOW + TOK_DEV, 0)
        return block_grads(q_blk, k_win, v_win, g_blk, q_docs, k_docs)

    attended, grad_q, key_terms, value_terms = lax.map(one_block, jnp.arange(pieces, dtype=jnp.int32))

    def accumulate(block_index, totals):
        first_row = (block_index * TOK_DEV).astype(jnp.int32)
        sum_k, sum_v = totals
        part_k = lax.dynamic_slice_in_dim(sum_k, first_row, WINDOW + TOK_DEV, 0) + key_terms[block_index].astype(jnp.float32)
        part_v = lax.dynamic_slice_in_dim(sum_v, first_row, WINDOW + TOK_DEV, 0) + value_terms[block_index].astype(jnp.float32)
        sum_k = lax.dynamic_update_slice_in_dim(sum_k, part_k, first_row, 0)
        sum_v = lax.dynamic_update_slice_in_dim(sum_v, part_v, first_row, 0)
        return (sum_k, sum_v)

    empty = jnp.zeros((pieces * TOK_DEV + WINDOW, KVH, HD), jnp.float32)
    sum_k, sum_v = lax.fori_loop(0, pieces, accumulate, (empty, empty))
    seq_rows = pieces * TOK_DEV
    return (attended.reshape(seq_rows, HQ, HD), grad_q.reshape(seq_rows, HQ, HD),
            sum_k[WINDOW:].astype(jnp.bfloat16), sum_v[WINDOW:].astype(jnp.bfloat16))
```

```python
import functools

import jax
import jax.numpy as jnp
from jax import lax
from jax.experimental import pallas as pl
from jax.experimental.pallas import tpu as pltpu
from jax.sharding import PartitionSpec as P

WINDOW = 1024


QUERY_SCALE = 168.0 ** (-0.5)

NT = (((1,), (1,)), ((), ()))
TN = (((0,), (0,)), ((), ()))


def shift(block, axis, distance):
    devices = range(lax.axis_size(axis))
    route = [(i, i + distance) for i in devices if i + distance in devices]
    return lax.ppermute(block, axis, route)


def to_sibling(block, axis, from_parity):
    size = lax.axis_size(axis)
    route = [(i, i ^ 1) for i in range(size) if i % 2 == from_parity]
    return lax.ppermute(block, axis, route)


def attention_kernel(qd_ref, kd_ref, q_ref, k_ref, v_ref, g_ref, o_ref, dq_ref, dk_ref, dv_ref):
    rows = q_ref.shape[0]
    cols = k_ref.shape[0]
    head_size = k_ref.shape[1]
    q_pos = lax.broadcasted_iota(jnp.int32, (rows, cols), 0)
    k_pos = lax.broadcasted_iota(jnp.int32, (rows, cols), 1)
    allowed = (qd_ref[...] == kd_ref[...]) & (k_pos > q_pos) & (k_pos <= q_pos + WINDOW)
    k = k_ref[...]
    v = v_ref[...]
    dk_acc = jnp.zeros((cols, head_size), jnp.float32)
    dv_acc = jnp.zeros((cols, head_size), jnp.float32)
    for a in range(q_ref.shape[1] // head_size):
        lanes = slice(a * head_size, (a + 1) * head_size)
        q = q_ref[:, lanes]
        g = g_ref[:, lanes]
        scores = QUERY_SCALE * lax.dot_general(q, k, NT, preferred_element_type=jnp.float32)
        masked = jnp.where(allowed, scores, -jnp.inf)
        row_max = jnp.max(masked, axis=1, keepdims=True)
        unnorm = jnp.exp(masked - row_max)
        inv = 1.0 / jnp.sum(unnorm, axis=1, keepdims=True)
        weights = unnorm * inv
        weights_b = weights.astype(jnp.bfloat16)
        attended = jnp.dot(weights_b, v, preferred_element_type=jnp.float32).astype(jnp.bfloat16)
        o_ref[:, lanes] = attended
        row_dot = jnp.sum(g.astype(jnp.float32) * attended.astype(jnp.float32), axis=1, keepdims=True)
        dprob = lax.dot_general(g, v, NT, preferred_element_type=jnp.float32)
        dscore = (weights * (dprob - row_dot)).astype(jnp.bfloat16)
        dq = QUERY_SCALE * jnp.dot(dscore, k, preferred_element_type=jnp.float32)
        dq_ref[:, lanes] = dq.astype(jnp.bfloat16)
        dk_acc = dk_acc + lax.dot_general(dscore, q, TN, preferred_element_type=jnp.float32)
        dv_acc = dv_acc + lax.dot_general(weights_b, g, TN, preferred_element_type=jnp.float32)
    dk_ref[...] = (QUERY_SCALE * dk_acc).astype(jnp.bfloat16)
    dv_ref[...] = dv_acc.astype(jnp.bfloat16)


def attention(q2, k_win, v_win, g2, q_docs, k_docs, groups, head_size):
    rows = q2.shape[0]
    cols = k_win.shape[0]
    per_group = q2.shape[1] // groups
    q_spec = pl.BlockSpec((rows, per_group), lambda i: (0, i))
    kv_spec = pl.BlockSpec((cols, head_size), lambda i: (0, i))
    flops = 12 * rows * cols * q2.shape[1]
    bytes_accessed = 2 * (4 * q2.size + 4 * k_win.size)
    return pl.pallas_call(
        attention_kernel,
        grid=(groups,),
        in_specs=[
            pl.BlockSpec((rows, 1), lambda i: (0, 0)),
            pl.BlockSpec((1, cols), lambda i: (0, 0)),
            q_spec,
            kv_spec,
            kv_spec,
            q_spec,
        ],
        out_specs=[q_spec, q_spec, kv_spec, kv_spec],
        out_shape=[
            jax.ShapeDtypeStruct(q2.shape, jnp.bfloat16),
            jax.ShapeDtypeStruct(q2.shape, jnp.bfloat16),
            jax.ShapeDtypeStruct(k_win.shape, jnp.bfloat16),
            jax.ShapeDtypeStruct(k_win.shape, jnp.bfloat16),
        ],
        compiler_params=pltpu.CompilerParams(dimension_semantics=("arbitrary",)),
        cost_estimate=pl.CostEstimate(
            flops=flops, transcendentals=rows * cols * q2.shape[1] // head_size,
            bytes_accessed=bytes_accessed),
    )(q_docs, k_docs, q2, k_win, v_win, g2)


def body(query_heads, key_heads, value_heads, grad_out, doc_ids):
    row_count = query_heads.shape[0]
    groups = key_heads.shape[1]
    head_size = key_heads.shape[2]
    reach = WINDOW // row_count
    assert reach == 4
    piece_pos = lax.axis_index("ctx")
    is_even = piece_pos % 2 == 0

    own = (key_heads, value_heads)
    back2 = shift(own, "ctx", 2)
    back4 = shift(back2, "ctx", 2)
    from_even_1 = to_sibling(own, "ctx", 0)
    from_odd_1 = to_sibling(back2, "ctx", 1)
    from_even_3 = to_sibling(back2, "ctx", 0)
    from_odd_3 = to_sibling(back4, "ctx", 1)
    back1 = jax.tree.map(lambda e, o: jnp.where(is_even, o, e), from_even_1, from_odd_1)
    back3 = jax.tree.map(lambda e, o: jnp.where(is_even, o, e), from_even_3, from_odd_3)
    pieces = [back4, back3, back2, back1, own]
    k_window = jnp.concatenate([p[0] for p in pieces], 0)
    v_window = jnp.concatenate([p[1] for p in pieces], 0)
    cols = k_window.shape[0]

    pad_docs = jnp.concatenate([jnp.full((WINDOW,), -1, jnp.int32), doc_ids], 0)
    first_row = piece_pos * row_count
    q_docs = lax.dynamic_slice_in_dim(doc_ids, first_row, row_count, 0)
    k_docs = lax.dynamic_slice_in_dim(pad_docs, first_row, WINDOW + row_count, 0)

    attended, grad_q, key_terms, value_terms = attention(
        query_heads.reshape(row_count, -1),
        k_window.reshape(cols, -1),
        v_window.reshape(cols, -1),
        grad_out.reshape(row_count, -1),
        q_docs.reshape(row_count, 1),
        k_docs.reshape(1, cols),
        groups,
        head_size,
    )
    key_terms = key_terms.reshape(cols, groups, head_size)
    value_terms = value_terms.reshape(cols, groups, head_size)

    def term_for(offset):
        lower = (reach - offset) * row_count
        return (key_terms[lower : lower + row_count], value_terms[lower : lower + row_count])

    def wide(pair):
        return tuple(x.astype(jnp.float32) for x in pair)

    def add(*pairs):
        total = wide(pairs[0])
        for pair in pairs[1:]:
            total = tuple(t + x.astype(jnp.float32) for t, x in zip(total, wide(pair)))
        return total

    def narrow(pair):
        return tuple(x.astype(jnp.bfloat16) for x in pair)

    terms = [term_for(d) for d in range(reach + 1)]
    sib = to_sibling((terms[1], terms[3]), "ctx", 0), to_sibling((terms[1], terms[3]), "ctx", 1)
    sib_1 = jax.tree.map(lambda e, o: jnp.where(is_even, o, e), sib[0][0], sib[1][0])
    sib_3 = jax.tree.map(lambda e, o: jnp.where(is_even, o, e), sib[0][1], sib[1][1])
    first = narrow(jax.tree.map(
        lambda p4, s3: jnp.where(is_even, p4.astype(jnp.float32), p4.astype(jnp.float32) + s3.astype(jnp.float32)),
        terms[4], sib_3))
    got_first = shift(first, "ctx", -2)
    second = narrow(jax.tree.map(
        lambda g, p2, s1, s3: g.astype(jnp.float32) + p2.astype(jnp.float32)
        + jnp.where(is_even, s3, s1).astype(jnp.float32),
        got_first, terms[2], sib_1, sib_3))
    got_second = shift(second, "ctx", -2)
    total = jax.tree.map(
        lambda g, p0, s1: g.astype(jnp.float32) + p0.astype(jnp.float32)
        + jnp.where(is_even, s1.astype(jnp.float32), 0.0),
        got_second, terms[0], sib_1)
    total_k, total_v = total
    attended = attended.reshape(query_heads.shape)
    grad_q = grad_q.reshape(query_heads.shape)
    return (attended, grad_q, total_k.astype(jnp.bfloat16), total_v.astype(jnp.bfloat16))


def solution(mesh):
    placed = (
        P(("dp", "ctx"), None, None),
        P(("dp", "ctx"), None, None),
        P(("dp", "ctx"), None, None),
        P(("dp", "ctx"), None, None),
        P("dp"),
    )
    return jax.shard_map(
        body,
        mesh=mesh,
        in_specs=placed,
        out_specs=(
            P(("dp", "ctx"), None, None),
            P(("dp", "ctx"), None, None),
            P(("dp", "ctx"), None, None),
            P(("dp", "ctx"), None, None),
        ),
        check_vma=False,
    )
```

```python
import jax
import jax.numpy as jnp
from jax import lax
from jax.experimental import pallas as pl
from jax.experimental.pallas import tpu as pltpu
from jax.sharding import PartitionSpec as P

WINDOW = 1024
CHUNKS = 1


QUERY_SCALE = 168.0 ** (-0.5)

NT = (((1,), (1,)), ((), ()))
TN = (((0,), (0,)), ((), ()))


def shift(block, axis, distance):
    devices = range(lax.axis_size(axis))
    route = [(i, i + distance) for i in devices if i + distance in devices]
    return lax.ppermute(block, axis, route)


def swap(block, axis):
    return lax.ppermute(block, axis, [(i, i ^ 1) for i in range(lax.axis_size(axis))])


def attention_kernel(qd_ref, kd_ref, q_ref, g_ref, p4_ref, p3_ref, p2_ref, p1_ref, p0_ref,
                     o_ref, dq_ref, d13_ref, d4_ref, d2_ref, d0_ref):
    rows = q_ref.shape[0]
    head_size = p0_ref.shape[2]
    pieces = (p4_ref, p3_ref, p2_ref, p1_ref, p0_ref)
    cols = rows * len(pieces)
    q_pos = lax.broadcasted_iota(jnp.int32, (rows, cols), 0)
    k_pos = lax.broadcasted_iota(jnp.int32, (rows, cols), 1)
    allowed = (qd_ref[...] == kd_ref[...]) & (k_pos > q_pos) & (k_pos <= q_pos + WINDOW)
    k = jnp.concatenate([p[0] for p in pieces], axis=0)
    v = jnp.concatenate([p[1] for p in pieces], axis=0)
    dk_acc = jnp.zeros((cols, head_size), jnp.float32)
    dv_acc = jnp.zeros((cols, head_size), jnp.float32)
    for a in range(q_ref.shape[1] // head_size):
        lanes = slice(a * head_size, (a + 1) * head_size)
        q = q_ref[:, lanes]
        g = g_ref[:, lanes]
        scores = QUERY_SCALE * lax.dot_general(q, k, NT, preferred_element_type=jnp.float32)
        masked = jnp.where(allowed, scores, -jnp.inf)
        row_max = jnp.max(masked, axis=1, keepdims=True)
        unnorm = jnp.exp(masked - row_max)
        inv = 1.0 / jnp.sum(unnorm, axis=1, keepdims=True)
        weights = unnorm * inv
        weights_b = weights.astype(jnp.bfloat16)
        attended = jnp.dot(weights_b, v, preferred_element_type=jnp.float32).astype(jnp.bfloat16)
        o_ref[:, lanes] = attended
        row_dot = jnp.sum(g.astype(jnp.float32) * attended.astype(jnp.float32), axis=1, keepdims=True)
        dprob = lax.dot_general(g, v, NT, preferred_element_type=jnp.float32)
        dscore = (weights * (dprob - row_dot)).astype(jnp.bfloat16)
        dq = QUERY_SCALE * jnp.dot(dscore, k, preferred_element_type=jnp.float32)
        dq_ref[:, lanes] = dq.astype(jnp.bfloat16)
        dk_acc = dk_acc + lax.dot_general(dscore, q, TN, preferred_element_type=jnp.float32)
        dv_acc = dv_acc + lax.dot_general(weights_b, g, TN, preferred_element_type=jnp.float32)
    for j, term in enumerate(((QUERY_SCALE * dk_acc).astype(jnp.bfloat16), dv_acc.astype(jnp.bfloat16))):
        d4_ref[j] = term[0:rows]
        d13_ref[j, rows:2 * rows] = term[rows:2 * rows]
        d2_ref[j] = term[2 * rows:3 * rows]
        d13_ref[j, 0:rows] = term[3 * rows:4 * rows]
        d0_ref[j] = term[4 * rows:5 * rows]


def attention(q2, g2, pieces, q_docs, k_docs, head_size):
    rows = q2.shape[0]
    groups = pieces[0].shape[2] // head_size
    per_group = q2.shape[1] // groups
    cols = rows * len(pieces)
    q_spec = pl.BlockSpec((rows, per_group), lambda i: (0, i))
    kv_spec = pl.BlockSpec((2, rows, head_size), lambda i: (0, 0, i))
    pair_spec = pl.BlockSpec((2, 2 * rows, head_size), lambda i: (0, 0, i))
    piece_shape = jax.ShapeDtypeStruct(pieces[0].shape, jnp.bfloat16)
    flops = 12 * rows * cols * q2.shape[1]
    bytes_accessed = 2 * (4 * q2.size + 10 * pieces[0].size)
    return pl.pallas_call(
        attention_kernel,
        grid=(groups,),
        in_specs=[
            pl.BlockSpec((rows, 1), lambda i: (0, 0)),
            pl.BlockSpec((1, cols), lambda i: (0, 0)),
            q_spec,
            q_spec,
        ] + [kv_spec] * len(pieces),
        out_specs=[q_spec, q_spec, pair_spec, kv_spec, kv_spec, kv_spec],
        out_shape=[
            jax.ShapeDtypeStruct(q2.shape, jnp.bfloat16),
            jax.ShapeDtypeStruct(q2.shape, jnp.bfloat16),
            jax.ShapeDtypeStruct((2, 2 * rows, pieces[0].shape[2]), jnp.bfloat16),
            piece_shape,
            piece_shape,
            piece_shape,
        ],
        compiler_params=pltpu.CompilerParams(dimension_semantics=("arbitrary",)),
        cost_estimate=pl.CostEstimate(
            flops=flops, transcendentals=rows * cols * q2.shape[1] // head_size,
            bytes_accessed=bytes_accessed),
    )(q_docs, k_docs, q2, g2, *pieces)


def wide(x):
    return x.astype(jnp.float32)


def chunk_grads(q2, g2, own, is_odd, q_docs, k_docs, head_size):
    rows = q2.shape[0]
    back2 = shift(own, "ctx", 2)
    back4 = shift(back2, "ctx", 2)
    back1 = swap(jnp.where(is_odd, back2, own), "ctx")
    back3 = swap(jnp.where(is_odd, back4, back2), "ctx")
    attended, grad_q, t13, t4, t2, t0 = attention(
        q2, g2, (back4, back3, back2, back1, own), q_docs, k_docs, head_size)
    s13 = swap(t13, "ctx")
    s1 = s13[:, :rows]
    s3 = s13[:, rows:]
    first = jnp.where(is_odd, wide(t4) + wide(s3), wide(t4)).astype(jnp.bfloat16)
    got1 = shift(first, "ctx", -2)
    second = (wide(got1) + wide(t2) + wide(jnp.where(is_odd, s1, s3))).astype(jnp.bfloat16)
    got2 = shift(second, "ctx", -2)
    total = wide(got2) + wide(t0) + jnp.where(is_odd, 0.0, wide(s1))
    return attended, grad_q, total


def body(query_heads, key_heads, value_heads, grad_out, doc_ids):
    row_count = query_heads.shape[0]
    groups = key_heads.shape[1]
    head_size = key_heads.shape[2]
    assert WINDOW // row_count == 4
    piece_pos = lax.axis_index("ctx")
    is_odd = piece_pos % 2 == 1

    pad_docs = jnp.concatenate([jnp.full((WINDOW,), -1, jnp.int32), doc_ids], 0)
    first_row = piece_pos * row_count
    q_docs = lax.dynamic_slice_in_dim(doc_ids, first_row, row_count, 0).reshape(row_count, 1)
    k_docs = lax.dynamic_slice_in_dim(pad_docs, first_row, WINDOW + row_count, 0).reshape(1, -1)

    q2 = query_heads.reshape(row_count, -1)
    g2 = grad_out.reshape(row_count, -1)
    kv = jnp.stack([key_heads.reshape(row_count, -1), value_heads.reshape(row_count, -1)])
    q_width = q2.shape[1] // CHUNKS
    kv_width = kv.shape[2] // CHUNKS
    results = []
    for c in range(CHUNKS):
        results.append(chunk_grads(
            q2[:, c * q_width:(c + 1) * q_width],
            g2[:, c * q_width:(c + 1) * q_width],
            kv[:, :, c * kv_width:(c + 1) * kv_width],
            is_odd, q_docs, k_docs, head_size))
    attended = jnp.concatenate([r[0] for r in results], 1).reshape(query_heads.shape)
    grad_q = jnp.concatenate([r[1] for r in results], 1).reshape(query_heads.shape)
    total = jnp.concatenate([r[2] for r in results], 2)
    grad_k = total[0].astype(jnp.bfloat16).reshape(key_heads.shape)
    grad_v = total[1].astype(jnp.bfloat16).reshape(value_heads.shape)
    return (attended, grad_q, grad_k, grad_v)


def solution(mesh):
    placed = (
        P(("dp", "ctx"), None, None),
        P(("dp", "ctx"), None, None),
        P(("dp", "ctx"), None, None),
        P(("dp", "ctx"), None, None),
        P("dp"),
    )
    return jax.shard_map(
        body,
        mesh=mesh,
        in_specs=placed,
        out_specs=(
            P(("dp", "ctx"), None, None),
            P(("dp", "ctx"), None, None),
            P(("dp", "ctx"), None, None),
            P(("dp", "ctx"), None, None),
        ),
        check_vma=False,
    )
```

```python
import jax
import jax.numpy as jnp
from jax import lax
from jax.experimental import pallas as pl
from jax.experimental.pallas import tpu as pltpu
from jax.sharding import PartitionSpec as P


WINDOW = 1024
CHUNKS = 4


QUERY_SCALE = 168.0 ** (-0.5)

NT = (((1,), (1,)), ((), ()))
TN = (((0,), (0,)), ((), ()))


def shift(block, axis, distance):
    devices = range(lax.axis_size(axis))
    route = [(i, i + distance) for i in devices if i + distance in devices]
    return lax.ppermute(block, axis, route)


def swap(block, axis):
    return lax.ppermute(block, axis, [(i, i ^ 1) for i in range(lax.axis_size(axis))])


def attention_kernel(qd_ref, kd_ref, q_ref, g_ref, p4_ref, p3_ref, p2_ref, p1_ref, p0_ref,
                     o_in, dq_in, o_ref, dq_ref, d13_ref, d4_ref, d2_ref, d0_ref):
    rows = q_ref.shape[0]
    head_size = p0_ref.shape[2]
    pieces = (p4_ref, p3_ref, p2_ref, p1_ref, p0_ref)
    cols = rows * len(pieces)
    q_pos = lax.broadcasted_iota(jnp.int32, (rows, cols), 0)
    k_pos = lax.broadcasted_iota(jnp.int32, (rows, cols), 1)
    allowed = (qd_ref[...] == kd_ref[...]) & (k_pos > q_pos) & (k_pos <= q_pos + WINDOW)
    k = jnp.concatenate([p[0] for p in pieces], axis=0)
    v = jnp.concatenate([p[1] for p in pieces], axis=0)
    dk_acc = jnp.zeros((cols, head_size), jnp.float32)
    dv_acc = jnp.zeros((cols, head_size), jnp.float32)
    for a in range(q_ref.shape[1] // head_size):
        lanes = slice(a * head_size, (a + 1) * head_size)
        q = q_ref[:, lanes]
        g = g_ref[:, lanes]
        scores = QUERY_SCALE * lax.dot_general(q, k, NT, preferred_element_type=jnp.float32)
        masked = jnp.where(allowed, scores, -jnp.inf)
        row_max = jnp.max(masked, axis=1, keepdims=True)
        unnorm = jnp.exp(masked - row_max)
        inv = 1.0 / jnp.sum(unnorm, axis=1, keepdims=True)
        weights = unnorm * inv
        weights_b = weights.astype(jnp.bfloat16)
        attended = jnp.dot(weights_b, v, preferred_element_type=jnp.float32).astype(jnp.bfloat16)
        o_ref[:, lanes] = attended
        row_dot = jnp.sum(g.astype(jnp.float32) * attended.astype(jnp.float32), axis=1, keepdims=True)
        dprob = lax.dot_general(g, v, NT, preferred_element_type=jnp.float32)
        dscore = (weights * (dprob - row_dot)).astype(jnp.bfloat16)
        dq = QUERY_SCALE * jnp.dot(dscore, k, preferred_element_type=jnp.float32)
        dq_ref[:, lanes] = dq.astype(jnp.bfloat16)
        dk_acc = dk_acc + lax.dot_general(dscore, q, TN, preferred_element_type=jnp.float32)
        dv_acc = dv_acc + lax.dot_general(weights_b, g, TN, preferred_element_type=jnp.float32)
    for j, term in enumerate(((QUERY_SCALE * dk_acc).astype(jnp.bfloat16), dv_acc.astype(jnp.bfloat16))):
        d4_ref[j] = term[0:rows]
        d13_ref[j, rows:2 * rows] = term[rows:2 * rows]
        d2_ref[j] = term[2 * rows:3 * rows]
        d13_ref[j, 0:rows] = term[3 * rows:4 * rows]
        d0_ref[j] = term[4 * rows:5 * rows]


def attention(q2, g2, pieces, q_docs, k_docs, head_size, chunk, o_buf, dq_buf):
    rows = q2.shape[0]
    groups = pieces[0].shape[2] // head_size
    per_group = 2 * head_size
    cols = rows * len(pieces)
    q_spec = pl.BlockSpec((rows, per_group), lambda i: (0, chunk * groups + i))
    kv_spec = pl.BlockSpec((2, rows, head_size), lambda i: (0, 0, i))
    pair_spec = pl.BlockSpec((2, 2 * rows, head_size), lambda i: (0, 0, i))
    piece_shape = jax.ShapeDtypeStruct(pieces[0].shape, jnp.bfloat16)
    flops = 12 * rows * cols * per_group * groups
    bytes_accessed = 2 * (4 * rows * per_group * groups + 10 * pieces[0].size)
    return pl.pallas_call(
        attention_kernel,
        grid=(groups,),
        in_specs=[
            pl.BlockSpec((rows, 1), lambda i: (0, 0)),
            pl.BlockSpec((1, cols), lambda i: (0, 0)),
            q_spec,
            q_spec,
        ] + [kv_spec] * len(pieces) + [pl.BlockSpec(memory_space=pl.ANY)] * 2,
        out_specs=[q_spec, q_spec, pair_spec, kv_spec, kv_spec, kv_spec],
        out_shape=[
            jax.ShapeDtypeStruct(q2.shape, jnp.bfloat16),
            jax.ShapeDtypeStruct(q2.shape, jnp.bfloat16),
            jax.ShapeDtypeStruct((2, 2 * rows, pieces[0].shape[2]), jnp.bfloat16),
            piece_shape,
            piece_shape,
            piece_shape,
        ],
        input_output_aliases={4 + len(pieces): 0, 5 + len(pieces): 1},
        compiler_params=pltpu.CompilerParams(dimension_semantics=("arbitrary",)),
        cost_estimate=pl.CostEstimate(
            flops=flops, transcendentals=rows * cols * per_group * groups // head_size,
            bytes_accessed=bytes_accessed),
    )(q_docs, k_docs, q2, g2, *pieces, o_buf, dq_buf)


def wide(x):
    return x.astype(jnp.float32)


def forward_exchange(own, is_odd):
    rows = own.shape[1]
    back2 = shift(own, "ctx", 2)
    back4 = shift(back2, "ctx", 2)
    odd_pieces = jnp.where(is_odd, jnp.concatenate([back2, back4], 1),
                           jnp.concatenate([own, back2], 1))
    back13 = swap(odd_pieces, "ctx")
    return (back4, back13[:, rows:], back2, back13[:, :rows], own)


def backward_exchange(terms, is_odd):
    t13, t4, t2, t0 = terms
    rows = t4.shape[1]
    s13 = swap(t13, "ctx")
    s1 = s13[:, :rows]
    s3 = s13[:, rows:]
    first = jnp.where(is_odd, wide(t4) + wide(s3), wide(t4)).astype(jnp.bfloat16)
    got1 = shift(first, "ctx", -2)
    second = (wide(got1) + wide(t2) + wide(jnp.where(is_odd, s1, s3))).astype(jnp.bfloat16)
    got2 = shift(second, "ctx", -2)
    return wide(got2) + wide(t0) + jnp.where(is_odd, 0.0, wide(s1))


def staged(query_heads, key_heads, value_heads, grad_out, doc_ids):
    row_count = query_heads.shape[0]
    head_size = key_heads.shape[2]
    assert WINDOW // row_count == 4
    piece_pos = lax.axis_index("ctx")
    is_odd = piece_pos % 2 == 1

    pad_docs = jnp.concatenate([jnp.full((WINDOW,), -1, jnp.int32), doc_ids], 0)
    first_row = piece_pos * row_count
    q_docs = lax.dynamic_slice_in_dim(doc_ids, first_row, row_count, 0).reshape(row_count, 1)
    k_docs = lax.dynamic_slice_in_dim(pad_docs, first_row, WINDOW + row_count, 0).reshape(1, -1)

    q2 = query_heads.reshape(row_count, -1)
    g2 = grad_out.reshape(row_count, -1)
    k2 = key_heads.reshape(row_count, -1)
    v2 = value_heads.reshape(row_count, -1)
    kv_width = k2.shape[1] // CHUNKS
    o_buf = jnp.zeros(q2.shape, jnp.bfloat16)
    dq_buf = jnp.zeros(q2.shape, jnp.bfloat16)
    totals = []
    for c in range(CHUNKS):
        lanes = slice(c * kv_width, (c + 1) * kv_width)
        own = jnp.stack([k2[:, lanes], v2[:, lanes]])
        pieces = forward_exchange(own, is_odd)
        o_buf, dq_buf, *terms = attention(
            q2, g2, pieces, q_docs, k_docs, head_size, c, o_buf, dq_buf)
        totals.append(backward_exchange(terms, is_odd))
    attended = o_buf.reshape(query_heads.shape)
    grad_q = dq_buf.reshape(query_heads.shape)
    total = jnp.concatenate(totals, 2)
    grad_k = total[0].astype(jnp.bfloat16).reshape(key_heads.shape)
    grad_v = total[1].astype(jnp.bfloat16).reshape(value_heads.shape)
    return (attended, grad_q, grad_k, grad_v)


def solution(mesh):
    placed = (
        P(("dp", "ctx"), None, None),
        P(("dp", "ctx"), None, None),
        P(("dp", "ctx"), None, None),
        P(("dp", "ctx"), None, None),
        P("dp"),
    )
    return jax.shard_map(
        staged,
        mesh=mesh,
        in_specs=placed,
        out_specs=(
            P(("dp", "ctx"), None, None),
            P(("dp", "ctx"), None, None),
            P(("dp", "ctx"), None, None),
            P(("dp", "ctx"), None, None),
        ),
        check_vma=False,
    )
```

```python
import jax
import jax.numpy as jnp
from jax import lax
from jax.experimental import pallas as pl
from jax.experimental.pallas import tpu as pltpu
from jax.sharding import PartitionSpec as P


WINDOW = 1024
CHUNKS = 4


QUERY_SCALE = 168.0 ** (-0.5)

NT = (((1,), (1,)), ((), ()))
TN = (((0,), (0,)), ((), ()))


def shift(block, axis, distance):
    size = lax.axis_size(axis)
    return lax.ppermute(block, axis, [(i, (i + distance) % size) for i in range(size)])


def swap(block, axis):
    return lax.ppermute(block, axis, [(i, i ^ 1) for i in range(lax.axis_size(axis))])


def attention_kernel(qd_ref, kd_ref, q_ref, g_ref, p4_ref, p3_ref, p2_ref, p1_ref, p0_ref,
                     o_in, dq_in, o_ref, dq_ref, d13_ref, d4_ref, d2_ref, d0_ref):
    rows = q_ref.shape[0]
    head_size = p0_ref.shape[2]
    pieces = (p4_ref, p3_ref, p2_ref, p1_ref, p0_ref)
    cols = rows * len(pieces)
    q_pos = lax.broadcasted_iota(jnp.int32, (rows, cols), 0)
    k_pos = lax.broadcasted_iota(jnp.int32, (rows, cols), 1)
    allowed = (qd_ref[...] == kd_ref[...]) & (k_pos > q_pos) & (k_pos <= q_pos + WINDOW)
    k = jnp.concatenate([p[0] for p in pieces], axis=0)
    v = jnp.concatenate([p[1] for p in pieces], axis=0)
    dk_acc = jnp.zeros((cols, head_size), jnp.float32)
    dv_acc = jnp.zeros((cols, head_size), jnp.float32)
    for a in range(q_ref.shape[1] // head_size):
        lanes = slice(a * head_size, (a + 1) * head_size)
        q = q_ref[:, lanes]
        g = g_ref[:, lanes]
        scores = QUERY_SCALE * lax.dot_general(q, k, NT, preferred_element_type=jnp.float32)
        masked = jnp.where(allowed, scores, -jnp.inf)
        row_max = jnp.max(masked, axis=1, keepdims=True)
        unnorm = jnp.exp(masked - row_max)
        inv = 1.0 / jnp.sum(unnorm, axis=1, keepdims=True)
        weights = unnorm * inv
        weights_b = weights.astype(jnp.bfloat16)
        attended = jnp.dot(weights_b, v, preferred_element_type=jnp.float32).astype(jnp.bfloat16)
        o_ref[:, lanes] = attended
        row_dot = jnp.sum(g.astype(jnp.float32) * attended.astype(jnp.float32), axis=1, keepdims=True)
        dprob = lax.dot_general(g, v, NT, preferred_element_type=jnp.float32)
        dscore = (weights * (dprob - row_dot)).astype(jnp.bfloat16)
        dq = QUERY_SCALE * jnp.dot(dscore, k, preferred_element_type=jnp.float32)
        dq_ref[:, lanes] = dq.astype(jnp.bfloat16)
        dk_acc = dk_acc + lax.dot_general(dscore, q, TN, preferred_element_type=jnp.float32)
        dv_acc = dv_acc + lax.dot_general(weights_b, g, TN, preferred_element_type=jnp.float32)
    for j, term in enumerate(((QUERY_SCALE * dk_acc).astype(jnp.bfloat16), dv_acc.astype(jnp.bfloat16))):
        d4_ref[j] = term[0:rows]
        d13_ref[j, rows:2 * rows] = term[rows:2 * rows]
        d2_ref[j] = term[2 * rows:3 * rows]
        d13_ref[j, 0:rows] = term[3 * rows:4 * rows]
        d0_ref[j] = term[4 * rows:5 * rows]


def attention(q2, g2, pieces, q_docs, k_docs, head_size, chunk, o_buf, dq_buf):
    rows = q2.shape[0]
    groups = pieces[0].shape[2] // head_size
    per_group = 2 * head_size
    cols = rows * len(pieces)
    q_spec = pl.BlockSpec((rows, per_group), lambda i: (0, chunk * groups + i))
    kv_spec = pl.BlockSpec((2, rows, head_size), lambda i: (0, 0, i))
    pair_spec = pl.BlockSpec((2, 2 * rows, head_size), lambda i: (0, 0, i))
    piece_shape = jax.ShapeDtypeStruct(pieces[0].shape, jnp.bfloat16)
    flops = 12 * rows * cols * per_group * groups
    bytes_accessed = 2 * (4 * rows * per_group * groups + 10 * pieces[0].size)
    return pl.pallas_call(
        attention_kernel,
        grid=(groups,),
        in_specs=[
            pl.BlockSpec((rows, 1), lambda i: (0, 0)),
            pl.BlockSpec((1, cols), lambda i: (0, 0)),
            q_spec,
            q_spec,
        ] + [kv_spec] * len(pieces) + [pl.BlockSpec(memory_space=pl.ANY)] * 2,
        out_specs=[q_spec, q_spec, pair_spec, kv_spec, kv_spec, kv_spec],
        out_shape=[
            jax.ShapeDtypeStruct(q2.shape, jnp.bfloat16),
            jax.ShapeDtypeStruct(q2.shape, jnp.bfloat16),
            jax.ShapeDtypeStruct((2, 2 * rows, pieces[0].shape[2]), jnp.bfloat16),
            piece_shape,
            piece_shape,
            piece_shape,
        ],
        input_output_aliases={4 + len(pieces): 0, 5 + len(pieces): 1},
        compiler_params=pltpu.CompilerParams(dimension_semantics=("arbitrary",)),
        cost_estimate=pl.CostEstimate(
            flops=flops, transcendentals=rows * cols * per_group * groups // head_size,
            bytes_accessed=bytes_accessed),
    )(q_docs, k_docs, q2, g2, *pieces, o_buf, dq_buf)


def wide(x):
    return x.astype(jnp.float32)


def forward_exchange(own, is_odd):
    rows = own.shape[1]
    back2 = shift(own, "ctx", 2)
    back4 = shift(back2, "ctx", 2)
    odd_pieces = jnp.where(is_odd, jnp.concatenate([back2, back4], 1),
                           jnp.concatenate([own, back2], 1))
    back13 = swap(odd_pieces, "ctx")
    return (back4, back13[:, rows:], back2, back13[:, :rows], own)


def backward_exchange(terms, is_odd):
    t13, t4, t2, t0 = terms
    rows = t4.shape[1]
    s13 = swap(t13, "ctx")
    s1 = s13[:, :rows]
    s3 = s13[:, rows:]
    first = jnp.where(is_odd, wide(t4) + wide(s3), wide(t4)).astype(jnp.bfloat16)
    got1 = shift(first, "ctx", -2)
    second = (wide(got1) + wide(t2) + wide(jnp.where(is_odd, s1, s3))).astype(jnp.bfloat16)
    got2 = shift(second, "ctx", -2)
    return wide(got2) + wide(t0) + jnp.where(is_odd, 0.0, wide(s1))


def staged(query_heads, key_heads, value_heads, grad_out, doc_ids):
    row_count = query_heads.shape[0]
    head_size = key_heads.shape[2]
    assert WINDOW // row_count == 4
    piece_pos = lax.axis_index("ctx")
    is_odd = piece_pos % 2 == 1

    pad_docs = jnp.concatenate([jnp.full((WINDOW,), -1, jnp.int32), doc_ids], 0)
    first_row = piece_pos * row_count
    q_docs = lax.dynamic_slice_in_dim(doc_ids, first_row, row_count, 0).reshape(row_count, 1)
    k_docs = lax.dynamic_slice_in_dim(pad_docs, first_row, WINDOW + row_count, 0).reshape(1, -1)

    q2 = query_heads.reshape(row_count, -1)
    g2 = grad_out.reshape(row_count, -1)
    k2 = key_heads.reshape(row_count, -1)
    v2 = value_heads.reshape(row_count, -1)
    kv_width = k2.shape[1] // CHUNKS
    o_buf = jnp.zeros(q2.shape, jnp.bfloat16)
    dq_buf = jnp.zeros(q2.shape, jnp.bfloat16)
    totals = []
    for c in range(CHUNKS):
        lanes = slice(c * kv_width, (c + 1) * kv_width)
        own = jnp.stack([k2[:, lanes], v2[:, lanes]])
        pieces = forward_exchange(own, is_odd)
        o_buf, dq_buf, *terms = attention(
            q2, g2, pieces, q_docs, k_docs, head_size, c, o_buf, dq_buf)
        totals.append(backward_exchange(terms, is_odd))
    attended = o_buf.reshape(query_heads.shape)
    grad_q = dq_buf.reshape(query_heads.shape)
    total = jnp.concatenate(totals, 2)
    grad_k = total[0].astype(jnp.bfloat16).reshape(key_heads.shape)
    grad_v = total[1].astype(jnp.bfloat16).reshape(value_heads.shape)
    return (attended, grad_q, grad_k, grad_v)


def solution(mesh):
    placed = (
        P(("dp", "ctx"), None, None),
        P(("dp", "ctx"), None, None),
        P(("dp", "ctx"), None, None),
        P(("dp", "ctx"), None, None),
        P("dp"),
    )
    return jax.shard_map(
        staged,
        mesh=mesh,
        in_specs=placed,
        out_specs=(
            P(("dp", "ctx"), None, None),
            P(("dp", "ctx"), None, None),
            P(("dp", "ctx"), None, None),
            P(("dp", "ctx"), None, None),
        ),
        check_vma=False,
    )
```

```python
import jax
import jax.numpy as jnp
from jax import lax
from jax.experimental import pallas as pl
from jax.experimental.pallas import tpu as pltpu
from jax.sharding import PartitionSpec as P


WINDOW = 1024
CHUNKS = 2


QUERY_SCALE = 168.0 ** (-0.5)

NT = (((1,), (1,)), ((), ()))
TN = (((0,), (0,)), ((), ()))


def shift(block, axis, distance):
    size = lax.axis_size(axis)
    return lax.ppermute(block, axis, [(i, (i + distance) % size) for i in range(size)])


def swap(block, axis):
    return lax.ppermute(block, axis, [(i, i ^ 1) for i in range(lax.axis_size(axis))])


def attention_kernel(qd_ref, kd_ref, q_ref, g_ref, p4_ref, p3_ref, p2_ref, p1_ref, p0_ref, *refs):
    o_ref, dq_ref, d13_ref, d4_ref, d2_ref, d0_ref = refs[-6:]
    rows = q_ref.shape[0]
    head_size = p0_ref.shape[2]
    pieces = (p4_ref, p3_ref, p2_ref, p1_ref, p0_ref)
    cols = rows * len(pieces)
    q_pos = lax.broadcasted_iota(jnp.int32, (rows, cols), 0)
    k_pos = lax.broadcasted_iota(jnp.int32, (rows, cols), 1)
    allowed = (qd_ref[...] == kd_ref[...]) & (k_pos > q_pos) & (k_pos <= q_pos + WINDOW)
    k = jnp.concatenate([p[0] for p in pieces], axis=0)
    v = jnp.concatenate([p[1] for p in pieces], axis=0)
    dk_acc = jnp.zeros((cols, head_size), jnp.float32)
    dv_acc = jnp.zeros((cols, head_size), jnp.float32)
    for a in range(q_ref.shape[1] // head_size):
        lanes = slice(a * head_size, (a + 1) * head_size)
        q = q_ref[:, lanes]
        g = g_ref[:, lanes]
        scores = QUERY_SCALE * lax.dot_general(q, k, NT, preferred_element_type=jnp.float32)
        masked = jnp.where(allowed, scores, -jnp.inf)
        row_max = jnp.max(masked, axis=1, keepdims=True)
        unnorm = jnp.exp(masked - row_max)
        inv = 1.0 / jnp.sum(unnorm, axis=1, keepdims=True)
        weights = unnorm * inv
        weights_b = weights.astype(jnp.bfloat16)
        attended = jnp.dot(weights_b, v, preferred_element_type=jnp.float32).astype(jnp.bfloat16)
        o_ref[:, lanes] = attended
        row_dot = jnp.sum(g.astype(jnp.float32) * attended.astype(jnp.float32), axis=1, keepdims=True)
        dprob = lax.dot_general(g, v, NT, preferred_element_type=jnp.float32)
        dscore = (weights * (dprob - row_dot)).astype(jnp.bfloat16)
        dq = QUERY_SCALE * jnp.dot(dscore, k, preferred_element_type=jnp.float32)
        dq_ref[:, lanes] = dq.astype(jnp.bfloat16)
        dk_acc = dk_acc + lax.dot_general(dscore, q, TN, preferred_element_type=jnp.float32)
        dv_acc = dv_acc + lax.dot_general(weights_b, g, TN, preferred_element_type=jnp.float32)
    for j, term in enumerate(((QUERY_SCALE * dk_acc).astype(jnp.bfloat16), dv_acc.astype(jnp.bfloat16))):
        d4_ref[j] = term[0:rows]
        d13_ref[j, rows:2 * rows] = term[rows:2 * rows]
        d2_ref[j] = term[2 * rows:3 * rows]
        d13_ref[j, 0:rows] = term[3 * rows:4 * rows]
        d0_ref[j] = term[4 * rows:5 * rows]


def attention(q2, g2, pieces, q_docs, k_docs, head_size, chunk, bufs):
    rows = q2.shape[0]
    groups = pieces[0].shape[2] // head_size
    per_group = 2 * head_size
    cols = rows * len(pieces)
    q_spec = pl.BlockSpec((rows, per_group), lambda i: (0, chunk * groups + i))
    kv_spec = pl.BlockSpec((2, rows, head_size), lambda i: (0, 0, i))
    pair_spec = pl.BlockSpec((2, 2 * rows, head_size), lambda i: (0, 0, i))
    piece_shape = jax.ShapeDtypeStruct(pieces[0].shape, jnp.bfloat16)
    flops = 12 * rows * cols * per_group * groups
    bytes_accessed = 2 * (4 * rows * per_group * groups + 10 * pieces[0].size)
    return pl.pallas_call(
        attention_kernel,
        grid=(groups,),
        in_specs=[
            pl.BlockSpec((rows, 1), lambda i: (0, 0)),
            pl.BlockSpec((1, cols), lambda i: (0, 0)),
            q_spec,
            q_spec,
        ] + [kv_spec] * len(pieces) + [pl.BlockSpec(memory_space=pl.ANY)] * len(bufs),
        out_specs=[q_spec, q_spec, pair_spec, kv_spec, kv_spec, kv_spec],
        out_shape=[
            jax.ShapeDtypeStruct(q2.shape, jnp.bfloat16),
            jax.ShapeDtypeStruct(q2.shape, jnp.bfloat16),
            jax.ShapeDtypeStruct((2, 2 * rows, pieces[0].shape[2]), jnp.bfloat16),
            piece_shape,
            piece_shape,
            piece_shape,
        ],
        input_output_aliases={4 + len(pieces) + j: j for j in range(len(bufs))},
        compiler_params=pltpu.CompilerParams(dimension_semantics=("arbitrary",)),
        cost_estimate=pl.CostEstimate(
            flops=flops, transcendentals=rows * cols * per_group * groups // head_size,
            bytes_accessed=bytes_accessed),
    )(q_docs, k_docs, q2, g2, *pieces, *bufs)


def wide(x):
    return x.astype(jnp.float32)


def forward_exchange(own, is_odd):
    rows = own.shape[1]
    back2 = shift(own, "ctx", 2)
    back4 = shift(back2, "ctx", 2)
    odd_pieces = jnp.where(is_odd, jnp.concatenate([back2, back4], 1),
                           jnp.concatenate([own, back2], 1))
    back13 = swap(odd_pieces, "ctx")
    return (back4, back13[:, rows:], back2, back13[:, :rows], own)


def backward_exchange(terms, is_odd):
    t13, t4, t2, t0 = terms
    rows = t4.shape[1]
    s13 = swap(t13, "ctx")
    s1 = s13[:, :rows]
    s3 = s13[:, rows:]
    first = jnp.where(is_odd, wide(t4) + wide(s3), wide(t4)).astype(jnp.bfloat16)
    got1 = shift(first, "ctx", -2)
    second = (wide(got1) + wide(t2) + wide(jnp.where(is_odd, s1, s3))).astype(jnp.bfloat16)
    got2 = shift(second, "ctx", -2)
    return wide(got2) + wide(t0) + jnp.where(is_odd, 0.0, wide(s1))


def staged(query_heads, key_heads, value_heads, grad_out, doc_ids):
    row_count = query_heads.shape[0]
    head_size = key_heads.shape[2]
    assert WINDOW // row_count == 4
    piece_pos = lax.axis_index("ctx")
    is_odd = piece_pos % 2 == 1

    pad_docs = jnp.concatenate([jnp.full((WINDOW,), -1, jnp.int32), doc_ids], 0)
    first_row = piece_pos * row_count
    q_docs = lax.dynamic_slice_in_dim(doc_ids, first_row, row_count, 0).reshape(row_count, 1)
    k_docs = lax.dynamic_slice_in_dim(pad_docs, first_row, WINDOW + row_count, 0).reshape(1, -1)
    q2 = query_heads.reshape(row_count, -1)
    g2 = grad_out.reshape(row_count, -1)
    k2 = key_heads.reshape(row_count, -1)
    v2 = value_heads.reshape(row_count, -1)
    kv_width = k2.shape[1] // CHUNKS
    bufs = ()
    totals = []
    for c in range(CHUNKS):
        lanes = slice(c * kv_width, (c + 1) * kv_width)
        own = jnp.stack([k2[:, lanes], v2[:, lanes]])
        pieces = forward_exchange(own, is_odd)
        o_buf, dq_buf, *terms = attention(
            q2, g2, pieces, q_docs, k_docs, head_size, c, bufs)
        bufs = (o_buf, dq_buf)
        totals.append(backward_exchange(terms, is_odd))
    attended = o_buf.reshape(query_heads.shape)
    grad_q = dq_buf.reshape(query_heads.shape)
    total = jnp.concatenate(totals, 2)
    grad_k = total[0].astype(jnp.bfloat16).reshape(key_heads.shape)
    grad_v = total[1].astype(jnp.bfloat16).reshape(value_heads.shape)
    return (attended, grad_q, grad_k, grad_v)


def solution(mesh):
    placed = (
        P(("dp", "ctx"), None, None),
        P(("dp", "ctx"), None, None),
        P(("dp", "ctx"), None, None),
        P(("dp", "ctx"), None, None),
        P("dp"),
    )
    return jax.shard_map(
        staged,
        mesh=mesh,
        in_specs=placed,
        out_specs=(
            P(("dp", "ctx"), None, None),
            P(("dp", "ctx"), None, None),
            P(("dp", "ctx"), None, None),
            P(("dp", "ctx"), None, None),
        ),
        check_vma=False,
    )
```

```python
import jax
import jax.numpy as jnp
from jax import lax
from jax.experimental import pallas as pl
from jax.experimental.pallas import tpu as pltpu
from jax.sharding import PartitionSpec as P


WINDOW = 1024
CHUNKS = 2


QUERY_SCALE = 168.0 ** (-0.5)

NT = (((1,), (1,)), ((), ()))
TN = (((0,), (0,)), ((), ()))


def shift(block, axis, distance):
    size = lax.axis_size(axis)
    return lax.ppermute(block, axis, [(i, (i + distance) % size) for i in range(size)])


def swap(block, axis):
    return lax.ppermute(block, axis, [(i, i ^ 1) for i in range(lax.axis_size(axis))])


def attention_kernel(flags_ref, qd_ref, kd_ref, q_ref, g_ref, p4_ref, p3_ref, p2_ref, p1_ref,
                     p0_ref, *refs):
    o_ref, dq_ref, d13_ref, d4_ref, d2_ref, d0_ref, s_scr, wb_scr, dk_scr, dv_scr = refs[-10:]
    rows = q_ref.shape[0]
    head_size = p0_ref.shape[2]
    pieces = (p4_ref, p3_ref, p2_ref, p1_ref, p0_ref)
    last = len(pieces) - 1
    dk_scr[...] = jnp.zeros_like(dk_scr)
    dv_scr[...] = jnp.zeros_like(dv_scr)

    def mask(j):
        allowed = qd_ref[...] == kd_ref[:, j * rows:(j + 1) * rows]
        q_pos = lax.broadcasted_iota(jnp.int32, (rows, rows), 0)
        k_pos = lax.broadcasted_iota(jnp.int32, (rows, rows), 1)
        if j == 0:
            allowed = allowed & (k_pos > q_pos)
        if j == last:
            allowed = allowed & (k_pos <= q_pos)
        return allowed

    def when(j, fn, keep):
        if j == last:
            return fn()
        return lax.cond(flags_ref[j] != 0, fn, lambda: keep)

    for a in range(q_ref.shape[1] // head_size):
        lanes = slice(a * head_size, (a + 1) * head_size)
        q = q_ref[:, lanes]
        g = g_ref[:, lanes]

        row_max = jnp.full((rows, 1), -jnp.inf, jnp.float32)
        for j in range(len(pieces)):
            def scores_of(j=j, row_max=row_max):
                scores = QUERY_SCALE * lax.dot_general(
                    q, pieces[j][0], NT, preferred_element_type=jnp.float32)
                masked = jnp.where(mask(j), scores, -jnp.inf)
                s_scr[j] = masked
                return jnp.maximum(row_max, jnp.max(masked, axis=1, keepdims=True))
            row_max = when(j, scores_of, row_max)

        total = jnp.zeros((rows, 1), jnp.float32)
        for j in range(len(pieces)):
            def exp_of(j=j, total=total):
                unnorm = jnp.exp(s_scr[j] - row_max)
                s_scr[j] = unnorm
                return total + jnp.sum(unnorm, axis=1, keepdims=True)
            total = when(j, exp_of, total)
        inv = 1.0 / total

        out = jnp.zeros((rows, head_size), jnp.float32)
        for j in range(len(pieces)):
            def attend(j=j, out=out):
                weights = s_scr[j] * inv
                s_scr[j] = weights
                weights_b = weights.astype(jnp.bfloat16)
                wb_scr[j] = weights_b
                return out + jnp.dot(weights_b, pieces[j][1], preferred_element_type=jnp.float32)
            out = when(j, attend, out)
        attended = out.astype(jnp.bfloat16)
        o_ref[:, lanes] = attended
        row_dot = jnp.sum(g.astype(jnp.float32) * attended.astype(jnp.float32), axis=1, keepdims=True)

        dq = jnp.zeros((rows, head_size), jnp.float32)
        for j in range(len(pieces)):
            def grads(j=j, dq=dq):
                dprob = lax.dot_general(g, pieces[j][1], NT, preferred_element_type=jnp.float32)
                dscore = (s_scr[j] * (dprob - row_dot)).astype(jnp.bfloat16)
                dk_scr[j] += lax.dot_general(dscore, q, TN, preferred_element_type=jnp.float32)
                dv_scr[j] += lax.dot_general(wb_scr[j], g, TN, preferred_element_type=jnp.float32)
                return dq + jnp.dot(dscore, pieces[j][0], preferred_element_type=jnp.float32)
            dq = when(j, grads, dq)
        dq_ref[:, lanes] = (QUERY_SCALE * dq).astype(jnp.bfloat16)

    for j, scr in enumerate((dk_scr, dv_scr)):
        scale = QUERY_SCALE if j == 0 else 1.0
        d4_ref[j] = (scale * scr[0]).astype(jnp.bfloat16)
        d13_ref[j, rows:2 * rows] = (scale * scr[1]).astype(jnp.bfloat16)
        d2_ref[j] = (scale * scr[2]).astype(jnp.bfloat16)
        d13_ref[j, 0:rows] = (scale * scr[3]).astype(jnp.bfloat16)
        d0_ref[j] = (scale * scr[4]).astype(jnp.bfloat16)


def attention(q2, g2, pieces, q_docs, k_docs, flags, head_size, chunk, bufs):
    rows = q2.shape[0]
    groups = pieces[0].shape[2] // head_size
    per_group = 2 * head_size
    cols = rows * len(pieces)
    q_spec = pl.BlockSpec((rows, per_group), lambda i, f: (0, chunk * groups + i))
    kv_spec = pl.BlockSpec((2, rows, head_size), lambda i, f: (0, 0, i))
    pair_spec = pl.BlockSpec((2, 2 * rows, head_size), lambda i, f: (0, 0, i))
    piece_shape = jax.ShapeDtypeStruct(pieces[0].shape, jnp.bfloat16)
    flops = 12 * rows * cols * per_group * groups
    bytes_accessed = 2 * (4 * rows * per_group * groups + 10 * pieces[0].size)
    return pl.pallas_call(
        attention_kernel,
        grid_spec=pltpu.PrefetchScalarGridSpec(
            num_scalar_prefetch=1,
            grid=(groups,),
            in_specs=[
                pl.BlockSpec((rows, 1), lambda i, f: (0, 0)),
                pl.BlockSpec((1, cols), lambda i, f: (0, 0)),
                q_spec,
                q_spec,
            ] + [kv_spec] * len(pieces) + [pl.BlockSpec(memory_space=pl.ANY)] * len(bufs),
            out_specs=[q_spec, q_spec, pair_spec, kv_spec, kv_spec, kv_spec],
            scratch_shapes=[
                pltpu.VMEM((len(pieces), rows, rows), jnp.float32),
                pltpu.VMEM((len(pieces), rows, rows), jnp.bfloat16),
                pltpu.VMEM((len(pieces), rows, head_size), jnp.float32),
                pltpu.VMEM((len(pieces), rows, head_size), jnp.float32),
            ],
        ),
        out_shape=[
            jax.ShapeDtypeStruct(q2.shape, jnp.bfloat16),
            jax.ShapeDtypeStruct(q2.shape, jnp.bfloat16),
            jax.ShapeDtypeStruct((2, 2 * rows, pieces[0].shape[2]), jnp.bfloat16),
            piece_shape,
            piece_shape,
            piece_shape,
        ],
        input_output_aliases={5 + len(pieces) + j: j for j in range(len(bufs))},
        compiler_params=pltpu.CompilerParams(dimension_semantics=("arbitrary",)),
        cost_estimate=pl.CostEstimate(
            flops=flops, transcendentals=rows * cols * per_group * groups // head_size,
            bytes_accessed=bytes_accessed),
    )(flags, q_docs, k_docs, q2, g2, *pieces, *bufs)


def wide(x):
    return x.astype(jnp.float32)


def forward_exchange(own, is_odd):
    rows = own.shape[1]
    back2 = shift(own, "ctx", 2)
    back4 = shift(back2, "ctx", 2)
    odd_pieces = jnp.where(is_odd, jnp.concatenate([back2, back4], 1),
                           jnp.concatenate([own, back2], 1))
    back13 = swap(odd_pieces, "ctx")
    return (back4, back13[:, rows:], back2, back13[:, :rows], own)


def backward_exchange(terms, is_odd):
    t13, t4, t2, t0 = terms
    rows = t4.shape[1]
    s13 = swap(t13, "ctx")
    s1 = s13[:, :rows]
    s3 = s13[:, rows:]
    first = jnp.where(is_odd, wide(t4) + wide(s3), wide(t4)).astype(jnp.bfloat16)
    got1 = shift(first, "ctx", -2)
    second = (wide(got1) + wide(t2) + wide(jnp.where(is_odd, s1, s3))).astype(jnp.bfloat16)
    got2 = shift(second, "ctx", -2)
    return wide(got2) + wide(t0) + jnp.where(is_odd, 0.0, wide(s1))


def staged(query_heads, key_heads, value_heads, grad_out, doc_ids):
    row_count = query_heads.shape[0]
    head_size = key_heads.shape[2]
    assert WINDOW // row_count == 4
    piece_pos = lax.axis_index("ctx")
    is_odd = piece_pos % 2 == 1

    pad_docs = jnp.concatenate([jnp.full((WINDOW,), -1, jnp.int32), doc_ids], 0)
    first_row = piece_pos * row_count
    q_docs = lax.dynamic_slice_in_dim(doc_ids, first_row, row_count, 0).reshape(row_count, 1)
    k_docs = lax.dynamic_slice_in_dim(pad_docs, first_row, WINDOW + row_count, 0).reshape(1, -1)
    ends = k_docs[0, row_count - 1:WINDOW:row_count]
    flags = (ends == q_docs[0, 0]).astype(jnp.int32)
    q2 = query_heads.reshape(row_count, -1)
    g2 = grad_out.reshape(row_count, -1)
    k2 = key_heads.reshape(row_count, -1)
    v2 = value_heads.reshape(row_count, -1)
    kv_width = k2.shape[1] // CHUNKS
    bufs = ()
    totals = []
    for c in range(CHUNKS):
        lanes = slice(c * kv_width, (c + 1) * kv_width)
        own = jnp.stack([k2[:, lanes], v2[:, lanes]])
        pieces = forward_exchange(own, is_odd)
        o_buf, dq_buf, *terms = attention(
            q2, g2, pieces, q_docs, k_docs, flags, head_size, c, bufs)
        bufs = (o_buf, dq_buf)
        totals.append(backward_exchange(terms, is_odd))
    attended = o_buf.reshape(query_heads.shape)
    grad_q = dq_buf.reshape(query_heads.shape)
    total = jnp.concatenate(totals, 2)
    grad_k = total[0].astype(jnp.bfloat16).reshape(key_heads.shape)
    grad_v = total[1].astype(jnp.bfloat16).reshape(value_heads.shape)
    return (attended, grad_q, grad_k, grad_v)


def solution(mesh):
    placed = (
        P(("dp", "ctx"), None, None),
        P(("dp", "ctx"), None, None),
        P(("dp", "ctx"), None, None),
        P(("dp", "ctx"), None, None),
        P("dp"),
    )
    return jax.shard_map(
        staged,
        mesh=mesh,
        in_specs=placed,
        out_specs=(
            P(("dp", "ctx"), None, None),
            P(("dp", "ctx"), None, None),
            P(("dp", "ctx"), None, None),
            P(("dp", "ctx"), None, None),
        ),
        check_vma=False,
    )
```

```python
import jax
import jax.numpy as jnp
from jax import lax
from jax.experimental import pallas as pl
from jax.experimental.pallas import tpu as pltpu
from jax.sharding import PartitionSpec as P


WINDOW = 1024
CHUNKS = 4


QUERY_SCALE = 168.0 ** (-0.5)

NT = (((1,), (1,)), ((), ()))
TN = (((0,), (0,)), ((), ()))


def shift(block, axis, distance):
    size = lax.axis_size(axis)
    return lax.ppermute(block, axis, [(i, (i + distance) % size) for i in range(size)])


def swap(block, axis):
    return lax.ppermute(block, axis, [(i, i ^ 1) for i in range(lax.axis_size(axis))])


def attention_kernel(qd_ref, kd_ref, q_ref, g_ref, p4_ref, p3_ref, p2_ref, p1_ref, p0_ref, *refs):
    o_ref, dq_ref, d13_ref, d4_ref, d2_ref, d0_ref = refs[-6:]
    rows = q_ref.shape[0]
    head_size = p0_ref.shape[2]
    pieces = (p4_ref, p3_ref, p2_ref, p1_ref, p0_ref)
    cols = rows * len(pieces)
    q_pos = lax.broadcasted_iota(jnp.int32, (rows, cols), 0)
    k_pos = lax.broadcasted_iota(jnp.int32, (rows, cols), 1)
    allowed = (qd_ref[...] == kd_ref[...]) & (k_pos > q_pos) & (k_pos <= q_pos + WINDOW)
    k = jnp.concatenate([p[0] for p in pieces], axis=0)
    v = jnp.concatenate([p[1] for p in pieces], axis=0)
    dk_acc = jnp.zeros((cols, head_size), jnp.float32)
    dv_acc = jnp.zeros((cols, head_size), jnp.float32)
    for a in range(q_ref.shape[1] // head_size):
        lanes = slice(a * head_size, (a + 1) * head_size)
        q = q_ref[:, lanes]
        g = g_ref[:, lanes]
        scores = QUERY_SCALE * lax.dot_general(q, k, NT, preferred_element_type=jnp.float32)
        masked = jnp.where(allowed, scores, -jnp.inf)
        row_max = jnp.max(masked, axis=1, keepdims=True)
        unnorm = jnp.exp(masked - row_max)
        inv = 1.0 / jnp.sum(unnorm, axis=1, keepdims=True)
        weights = unnorm * inv
        weights_b = weights.astype(jnp.bfloat16)
        attended = jnp.dot(weights_b, v, preferred_element_type=jnp.float32).astype(jnp.bfloat16)
        o_ref[:, lanes] = attended
        row_dot = jnp.sum(g.astype(jnp.float32) * attended.astype(jnp.float32), axis=1, keepdims=True)
        dprob = lax.dot_general(g, v, NT, preferred_element_type=jnp.float32)
        dscore = (weights * (dprob - row_dot)).astype(jnp.bfloat16)
        dq = QUERY_SCALE * jnp.dot(dscore, k, preferred_element_type=jnp.float32)
        dq_ref[:, lanes] = dq.astype(jnp.bfloat16)
        dk_acc = dk_acc + lax.dot_general(dscore, q, TN, preferred_element_type=jnp.float32)
        dv_acc = dv_acc + lax.dot_general(weights_b, g, TN, preferred_element_type=jnp.float32)
    for j, term in enumerate(((QUERY_SCALE * dk_acc).astype(jnp.bfloat16), dv_acc.astype(jnp.bfloat16))):
        d4_ref[j] = term[0:rows]
        d13_ref[j, rows:2 * rows] = term[rows:2 * rows]
        d2_ref[j] = term[2 * rows:3 * rows]
        d13_ref[j, 0:rows] = term[3 * rows:4 * rows]
        d0_ref[j] = term[4 * rows:5 * rows]


def attention(q2, g2, pieces, q_docs, k_docs, head_size, chunk, bufs):
    rows = q2.shape[0]
    pieces, blocks = zip(*pieces)
    groups = pieces[0].shape[2] // head_size
    per_group = 2 * head_size
    cols = rows * len(pieces)
    q_spec = pl.BlockSpec((rows, per_group), lambda i: (0, chunk * groups + i))
    kv_spec = pl.BlockSpec((2, rows, head_size), lambda i: (0, 0, i))
    pair_spec = pl.BlockSpec((2, 2 * rows, head_size), lambda i: (0, 0, i))
    piece_shape = jax.ShapeDtypeStruct(pieces[-1].shape, jnp.bfloat16)
    flops = 12 * rows * cols * per_group * groups
    bytes_accessed = 2 * (4 * rows * per_group * groups + 10 * pieces[-1].size)
    return pl.pallas_call(
        attention_kernel,
        grid=(groups,),
        in_specs=[
            pl.BlockSpec((rows, 1), lambda i: (0, 0)),
            pl.BlockSpec((1, cols), lambda i: (0, 0)),
            q_spec,
            q_spec,
        ] + [pl.BlockSpec((2, rows, head_size), lambda i, b=b: (0, b, i)) for b in blocks]
        + [pl.BlockSpec(memory_space=pl.ANY)] * len(bufs),
        out_specs=[q_spec, q_spec, pair_spec, kv_spec, kv_spec, kv_spec],
        out_shape=[
            jax.ShapeDtypeStruct(q2.shape, jnp.bfloat16),
            jax.ShapeDtypeStruct(q2.shape, jnp.bfloat16),
            jax.ShapeDtypeStruct((2, 2 * rows, pieces[0].shape[2]), jnp.bfloat16),
            piece_shape,
            piece_shape,
            piece_shape,
        ],
        input_output_aliases={4 + len(pieces) + j: j for j in range(len(bufs))},
        compiler_params=pltpu.CompilerParams(dimension_semantics=("arbitrary",)),
        cost_estimate=pl.CostEstimate(
            flops=flops, transcendentals=rows * cols * per_group * groups // head_size,
            bytes_accessed=bytes_accessed),
    )(q_docs, k_docs, q2, g2, *pieces, *bufs)


def wide(x):
    return x.astype(jnp.float32)


def forward_exchange(own, is_odd):
    back2 = shift(own, "ctx", 2)
    back4 = shift(back2, "ctx", 2)
    odd_pieces = jnp.where(is_odd, jnp.concatenate([back2, back4], 1),
                           jnp.concatenate([own, back2], 1))
    back13 = swap(odd_pieces, "ctx")
    return ((back4, 0), (back13, 1), (back2, 0), (back13, 0), (own, 0))


def backward_exchange(terms, is_odd):
    t13, t4, t2, t0 = terms
    rows = t4.shape[1]
    s13 = swap(t13, "ctx")
    s1 = s13[:, :rows]
    s3 = s13[:, rows:]
    first = jnp.where(is_odd, wide(t4) + wide(s3), wide(t4)).astype(jnp.bfloat16)
    got1 = shift(first, "ctx", -2)
    second = (wide(got1) + wide(t2) + wide(jnp.where(is_odd, s1, s3))).astype(jnp.bfloat16)
    got2 = shift(second, "ctx", -2)
    return wide(got2) + wide(t0) + jnp.where(is_odd, 0.0, wide(s1))


def staged(query_heads, key_heads, value_heads, grad_out, doc_ids):
    row_count = query_heads.shape[0]
    head_size = key_heads.shape[2]
    assert WINDOW // row_count == 4
    piece_pos = lax.axis_index("ctx")
    is_odd = piece_pos % 2 == 1

    pad_docs = jnp.concatenate([jnp.full((WINDOW,), -1, jnp.int32), doc_ids], 0)
    first_row = piece_pos * row_count
    q_docs = lax.dynamic_slice_in_dim(doc_ids, first_row, row_count, 0).reshape(row_count, 1)
    k_docs = lax.dynamic_slice_in_dim(pad_docs, first_row, WINDOW + row_count, 0).reshape(1, -1)
    q2 = query_heads.reshape(row_count, -1)
    g2 = grad_out.reshape(row_count, -1)
    k2 = key_heads.reshape(row_count, -1)
    v2 = value_heads.reshape(row_count, -1)
    kv_width = k2.shape[1] // CHUNKS
    bufs = ()
    totals = []
    for c in range(CHUNKS):
        lanes = slice(c * kv_width, (c + 1) * kv_width)
        own = jnp.stack([k2[:, lanes], v2[:, lanes]])
        pieces = forward_exchange(own, is_odd)
        o_buf, dq_buf, *terms = attention(
            q2, g2, pieces, q_docs, k_docs, head_size, c, bufs)
        bufs = (o_buf, dq_buf)
        totals.append(backward_exchange(terms, is_odd))
    attended = o_buf.reshape(query_heads.shape)
    grad_q = dq_buf.reshape(query_heads.shape)
    total = jnp.concatenate(totals, 2)
    grad_k = total[0].astype(jnp.bfloat16).reshape(key_heads.shape)
    grad_v = total[1].astype(jnp.bfloat16).reshape(value_heads.shape)
    return (attended, grad_q, grad_k, grad_v)


def solution(mesh):
    placed = (
        P(("dp", "ctx"), None, None),
        P(("dp", "ctx"), None, None),
        P(("dp", "ctx"), None, None),
        P(("dp", "ctx"), None, None),
        P("dp"),
    )
    return jax.shard_map(
        staged,
        mesh=mesh,
        in_specs=placed,
        out_specs=(
            P(("dp", "ctx"), None, None),
            P(("dp", "ctx"), None, None),
            P(("dp", "ctx"), None, None),
            P(("dp", "ctx"), None, None),
        ),
        check_vma=False,
    )
```

```python
import jax
import jax.numpy as jnp
from jax import lax
from jax.experimental import pallas as pl
from jax.experimental.pallas import tpu as pltpu
from jax.sharding import PartitionSpec as P


WINDOW = 1024
CHUNKS = 2


QUERY_SCALE = 168.0 ** (-0.5)

NT = (((1,), (1,)), ((), ()))
TN = (((0,), (0,)), ((), ()))


def shift(block, axis, distance):
    size = lax.axis_size(axis)
    return lax.ppermute(block, axis, [(i, (i + distance) % size) for i in range(size)])


def swap(block, axis):
    return lax.ppermute(block, axis, [(i, i ^ 1) for i in range(lax.axis_size(axis))])


def attention_kernel(bias_ref, q_ref, g_ref, p4_ref, p3_ref, p2_ref, p1_ref, p0_ref, *refs):
    o_ref, dq_ref, d13_ref, d4_ref, d2_ref, d0_ref = refs[-6:]
    rows = q_ref.shape[0]
    head_size = p0_ref.shape[2]
    pieces = (p4_ref, p3_ref, p2_ref, p1_ref, p0_ref)
    k = jnp.concatenate([p[0] for p in pieces], axis=0)
    v = jnp.concatenate([p[1] for p in pieces], axis=0)
    heads = q_ref.shape[1] // head_size
    q = jnp.concatenate([q_ref[:, a * head_size:(a + 1) * head_size] for a in range(heads)], 0)
    g = jnp.concatenate([g_ref[:, a * head_size:(a + 1) * head_size] for a in range(heads)], 0)
    scores = QUERY_SCALE * lax.dot_general(q, k, NT, preferred_element_type=jnp.float32)
    masked = scores + bias_ref[...]
    row_max = jnp.max(masked, axis=1, keepdims=True)
    unnorm = jnp.exp(masked - row_max)
    inv = 1.0 / jnp.sum(unnorm, axis=1, keepdims=True)
    weights = unnorm * inv
    weights_b = weights.astype(jnp.bfloat16)
    attended = jnp.dot(weights_b, v, preferred_element_type=jnp.float32).astype(jnp.bfloat16)
    row_dot = jnp.sum(g.astype(jnp.float32) * attended.astype(jnp.float32), axis=1, keepdims=True)
    dprob = lax.dot_general(g, v, NT, preferred_element_type=jnp.float32)
    dscore = (weights * (dprob - row_dot)).astype(jnp.bfloat16)
    dq = (QUERY_SCALE * jnp.dot(dscore, k, preferred_element_type=jnp.float32)).astype(jnp.bfloat16)
    for a in range(heads):
        o_ref[:, a * head_size:(a + 1) * head_size] = attended[a * rows:(a + 1) * rows]
        dq_ref[:, a * head_size:(a + 1) * head_size] = dq[a * rows:(a + 1) * rows]
    dk_acc = lax.dot_general(dscore, q, TN, preferred_element_type=jnp.float32)
    dv_acc = lax.dot_general(weights_b, g, TN, preferred_element_type=jnp.float32)
    for j, term in enumerate(((QUERY_SCALE * dk_acc).astype(jnp.bfloat16), dv_acc.astype(jnp.bfloat16))):
        d4_ref[j] = term[0:rows]
        d13_ref[j, rows:2 * rows] = term[rows:2 * rows]
        d2_ref[j] = term[2 * rows:3 * rows]
        d13_ref[j, 0:rows] = term[3 * rows:4 * rows]
        d0_ref[j] = term[4 * rows:5 * rows]


def attention(q2, g2, pieces, bias, head_size, chunk, bufs):
    rows = q2.shape[0]
    pieces, blocks = zip(*pieces)
    groups = pieces[0].shape[2] // head_size
    per_group = 2 * head_size
    cols = rows * len(pieces)
    q_spec = pl.BlockSpec((rows, per_group), lambda i: (0, chunk * groups + i))
    kv_spec = pl.BlockSpec((2, rows, head_size), lambda i: (0, 0, i))
    pair_spec = pl.BlockSpec((2, 2 * rows, head_size), lambda i: (0, 0, i))
    piece_shape = jax.ShapeDtypeStruct(pieces[-1].shape, jnp.bfloat16)
    flops = 12 * rows * cols * per_group * groups
    bytes_accessed = 2 * (4 * rows * per_group * groups + 10 * pieces[-1].size)
    return pl.pallas_call(
        attention_kernel,
        grid=(groups,),
        in_specs=[
            pl.BlockSpec(bias.shape, lambda i: (0, 0)),
            q_spec,
            q_spec,
        ] + [pl.BlockSpec((2, rows, head_size), lambda i, b=b: (0, b, i)) for b in blocks]
        + [pl.BlockSpec(memory_space=pl.ANY)] * len(bufs),
        out_specs=[q_spec, q_spec, pair_spec, kv_spec, kv_spec, kv_spec],
        out_shape=[
            jax.ShapeDtypeStruct(q2.shape, jnp.bfloat16),
            jax.ShapeDtypeStruct(q2.shape, jnp.bfloat16),
            jax.ShapeDtypeStruct((2, 2 * rows, pieces[0].shape[2]), jnp.bfloat16),
            piece_shape,
            piece_shape,
            piece_shape,
        ],
        input_output_aliases={3 + len(pieces) + j: j for j in range(len(bufs))},
        compiler_params=pltpu.CompilerParams(dimension_semantics=("arbitrary",)),
        cost_estimate=pl.CostEstimate(
            flops=flops, transcendentals=rows * cols * per_group * groups // head_size,
            bytes_accessed=bytes_accessed),
    )(bias, q2, g2, *pieces, *bufs)


def wide(x):
    return x.astype(jnp.float32)


def forward_exchange(own, is_odd):
    back2 = shift(own, "ctx", 2)
    back4 = shift(back2, "ctx", 2)
    odd_pieces = jnp.where(is_odd, jnp.concatenate([back2, back4], 1),
                           jnp.concatenate([own, back2], 1))
    back13 = swap(odd_pieces, "ctx")
    return ((back4, 0), (back13, 1), (back2, 0), (back13, 0), (own, 0))


def backward_exchange(terms, is_odd):
    t13, t4, t2, t0 = terms
    rows = t4.shape[1]
    s13 = swap(t13, "ctx")
    s1 = s13[:, :rows]
    s3 = s13[:, rows:]
    first = jnp.where(is_odd, wide(t4) + wide(s3), wide(t4)).astype(jnp.bfloat16)
    got1 = shift(first, "ctx", -2)
    second = (wide(got1) + wide(t2) + wide(jnp.where(is_odd, s1, s3))).astype(jnp.bfloat16)
    got2 = shift(second, "ctx", -2)
    return wide(got2) + wide(t0) + jnp.where(is_odd, 0.0, wide(s1))


def staged(query_heads, key_heads, value_heads, grad_out, doc_ids):
    row_count = query_heads.shape[0]
    groups = key_heads.shape[1]
    head_size = key_heads.shape[2]
    assert WINDOW // row_count == 4
    piece_pos = lax.axis_index("ctx")
    is_odd = piece_pos % 2 == 1

    pad_docs = jnp.concatenate([jnp.full((WINDOW,), -1, jnp.int32), doc_ids], 0)
    first_row = piece_pos * row_count
    q_docs = lax.dynamic_slice_in_dim(doc_ids, first_row, row_count, 0).reshape(row_count, 1)
    k_docs = lax.dynamic_slice_in_dim(pad_docs, first_row, WINDOW + row_count, 0).reshape(1, -1)
    cols = k_docs.shape[1]
    q_pos = lax.broadcasted_iota(jnp.int32, (row_count, cols), 0)
    k_pos = lax.broadcasted_iota(jnp.int32, (row_count, cols), 1)
    allowed = (q_docs == k_docs) & (k_pos > q_pos) & (k_pos <= q_pos + WINDOW)
    bias = jnp.where(allowed, 0.0, -jnp.inf).astype(jnp.float32)
    bias = jnp.concatenate([bias] * (query_heads.shape[1] // groups), 0)
    q2 = query_heads.reshape(row_count, -1)
    g2 = grad_out.reshape(row_count, -1)
    k2 = key_heads.reshape(row_count, -1)
    v2 = value_heads.reshape(row_count, -1)
    kv_width = k2.shape[1] // CHUNKS
    bufs = ()
    totals = []
    for c in range(CHUNKS):
        lanes = slice(c * kv_width, (c + 1) * kv_width)
        own = jnp.stack([k2[:, lanes], v2[:, lanes]])
        pieces = forward_exchange(own, is_odd)
        o_buf, dq_buf, *terms = attention(
            q2, g2, pieces, bias, head_size, c, bufs)
        bufs = (o_buf, dq_buf)
        totals.append(backward_exchange(terms, is_odd))
    attended = o_buf.reshape(query_heads.shape)
    grad_q = dq_buf.reshape(query_heads.shape)
    total = jnp.concatenate(totals, 2)
    grad_k = total[0].astype(jnp.bfloat16).reshape(key_heads.shape)
    grad_v = total[1].astype(jnp.bfloat16).reshape(value_heads.shape)
    return (attended, grad_q, grad_k, grad_v)


def solution(mesh):
    placed = (
        P(("dp", "ctx"), None, None),
        P(("dp", "ctx"), None, None),
        P(("dp", "ctx"), None, None),
        P(("dp", "ctx"), None, None),
        P("dp"),
    )
    return jax.shard_map(
        staged,
        mesh=mesh,
        in_specs=placed,
        out_specs=(
            P(("dp", "ctx"), None, None),
            P(("dp", "ctx"), None, None),
            P(("dp", "ctx"), None, None),
            P(("dp", "ctx"), None, None),
        ),
        check_vma=False,
    )
```

```python
import jax
import jax.numpy as jnp
from jax import lax
from jax.experimental import pallas as pl
from jax.experimental.pallas import tpu as pltpu
from jax.sharding import PartitionSpec as P


WINDOW = 1024
CHUNKS = 2


QUERY_SCALE = 168.0 ** (-0.5)

NT = (((1,), (1,)), ((), ()))
TN = (((0,), (0,)), ((), ()))


def shift(block, axis, distance):
    size = lax.axis_size(axis)
    return lax.ppermute(block, axis, [(i, (i + distance) % size) for i in range(size)])


def swap(block, axis):
    return lax.ppermute(block, axis, [(i, i ^ 1) for i in range(lax.axis_size(axis))])


def attention_kernel(qd_ref, kd_ref, q_ref, g_ref, p4_ref, p3_ref, p2_ref, p1_ref, p0_ref, *refs):
    o_ref, dq_ref, d13_ref, d4_ref, d2_ref, d0_ref = refs[-6:]
    rows = q_ref.shape[0]
    head_size = p0_ref.shape[2]
    pieces = (p4_ref, p3_ref, p2_ref, p1_ref, p0_ref)
    cols = rows * len(pieces)
    q_pos = lax.broadcasted_iota(jnp.int32, (rows, cols), 0)
    k_pos = lax.broadcasted_iota(jnp.int32, (rows, cols), 1)
    allowed = (qd_ref[...] == kd_ref[...]) & (k_pos > q_pos) & (k_pos <= q_pos + WINDOW)
    k = jnp.concatenate([p[0] for p in pieces], axis=0)
    v = jnp.concatenate([p[1] for p in pieces], axis=0)
    heads = q_ref.shape[1] // head_size
    q = jnp.concatenate([q_ref[:, a * head_size:(a + 1) * head_size] for a in range(heads)], 0)
    g = jnp.concatenate([g_ref[:, a * head_size:(a + 1) * head_size] for a in range(heads)], 0)
    allowed = jnp.concatenate([allowed] * heads, 0)
    scores = QUERY_SCALE * lax.dot_general(q, k, NT, preferred_element_type=jnp.float32)
    masked = jnp.where(allowed, scores, -jnp.inf)
    row_max = jnp.max(masked, axis=1, keepdims=True)
    unnorm = jnp.exp(masked - row_max)
    inv = 1.0 / jnp.sum(unnorm, axis=1, keepdims=True)
    weights = unnorm * inv
    weights_b = weights.astype(jnp.bfloat16)
    attended = jnp.dot(weights_b, v, preferred_element_type=jnp.float32).astype(jnp.bfloat16)
    row_dot = jnp.sum(g.astype(jnp.float32) * attended.astype(jnp.float32), axis=1, keepdims=True)
    dprob = lax.dot_general(g, v, NT, preferred_element_type=jnp.float32)
    dscore = (weights * (dprob - row_dot)).astype(jnp.bfloat16)
    dq = (QUERY_SCALE * jnp.dot(dscore, k, preferred_element_type=jnp.float32)).astype(jnp.bfloat16)
    for a in range(heads):
        o_ref[:, a * head_size:(a + 1) * head_size] = attended[a * rows:(a + 1) * rows]
        dq_ref[:, a * head_size:(a + 1) * head_size] = dq[a * rows:(a + 1) * rows]
    dk_acc = lax.dot_general(dscore, q, TN, preferred_element_type=jnp.float32)
    dv_acc = lax.dot_general(weights_b, g, TN, preferred_element_type=jnp.float32)
    for j, term in enumerate(((QUERY_SCALE * dk_acc).astype(jnp.bfloat16), dv_acc.astype(jnp.bfloat16))):
        d4_ref[j] = term[0:rows]
        d13_ref[j, rows:2 * rows] = term[rows:2 * rows]
        d2_ref[j] = term[2 * rows:3 * rows]
        d13_ref[j, 0:rows] = term[3 * rows:4 * rows]
        d0_ref[j] = term[4 * rows:5 * rows]


def attention(q2, g2, pieces, q_docs, k_docs, head_size, chunk, bufs):
    rows = q2.shape[0]
    pieces, blocks = zip(*pieces)
    groups = pieces[0].shape[2] // head_size
    per_group = 2 * head_size
    cols = rows * len(pieces)
    q_spec = pl.BlockSpec((rows, per_group), lambda i: (0, chunk * groups + i))
    kv_spec = pl.BlockSpec((2, rows, head_size), lambda i: (0, 0, i))
    pair_spec = pl.BlockSpec((2, 2 * rows, head_size), lambda i: (0, 0, i))
    piece_shape = jax.ShapeDtypeStruct(pieces[-1].shape, jnp.bfloat16)
    flops = 12 * rows * cols * per_group * groups
    bytes_accessed = 2 * (4 * rows * per_group * groups + 10 * pieces[-1].size)
    return pl.pallas_call(
        attention_kernel,
        grid=(groups,),
        in_specs=[
            pl.BlockSpec((rows, 1), lambda i: (0, 0)),
            pl.BlockSpec((1, cols), lambda i: (0, 0)),
            q_spec,
            q_spec,
        ] + [pl.BlockSpec((2, rows, head_size), lambda i, b=b: (0, b, i)) for b in blocks]
        + [pl.BlockSpec(memory_space=pl.ANY)] * len(bufs),
        out_specs=[q_spec, q_spec, pair_spec, kv_spec, kv_spec, kv_spec],
        out_shape=[
            jax.ShapeDtypeStruct(q2.shape, jnp.bfloat16),
            jax.ShapeDtypeStruct(q2.shape, jnp.bfloat16),
            jax.ShapeDtypeStruct((2, 2 * rows, pieces[0].shape[2]), jnp.bfloat16),
            piece_shape,
            piece_shape,
            piece_shape,
        ],
        input_output_aliases={4 + len(pieces) + j: j for j in range(len(bufs))},
        compiler_params=pltpu.CompilerParams(
            dimension_semantics=("arbitrary",)),
        cost_estimate=pl.CostEstimate(
            flops=flops, transcendentals=rows * cols * per_group * groups // head_size,
            bytes_accessed=bytes_accessed),
    )(q_docs, k_docs, q2, g2, *pieces, *bufs)


def wide(x):
    return x.astype(jnp.float32)


def forward_exchange(own, is_odd):
    back2 = shift(own, "ctx", 2)
    back4 = shift(back2, "ctx", 2)
    odd_pieces = jnp.where(is_odd, jnp.concatenate([back2, back4], 1),
                           jnp.concatenate([own, back2], 1))
    back13 = swap(odd_pieces, "ctx")
    return ((back4, 0), (back13, 1), (back2, 0), (back13, 0), (own, 0))


def backward_exchange(terms, is_odd):
    t13, t4, t2, t0 = terms
    rows = t4.shape[1]
    s13 = swap(t13, "ctx")
    s1 = s13[:, :rows]
    s3 = s13[:, rows:]
    first = jnp.where(is_odd, wide(t4) + wide(s3), wide(t4)).astype(jnp.bfloat16)
    got1 = shift(first, "ctx", -2)
    second = (wide(got1) + wide(t2) + wide(jnp.where(is_odd, s1, s3))).astype(jnp.bfloat16)
    got2 = shift(second, "ctx", -2)
    return wide(got2) + wide(t0) + jnp.where(is_odd, 0.0, wide(s1))


def staged(query_heads, key_heads, value_heads, grad_out, doc_ids):
    row_count = query_heads.shape[0]
    head_size = key_heads.shape[2]
    assert WINDOW // row_count == 4
    piece_pos = lax.axis_index("ctx")
    is_odd = piece_pos % 2 == 1

    pad_docs = jnp.concatenate([jnp.full((WINDOW,), -1, jnp.int32), doc_ids], 0)
    first_row = piece_pos * row_count
    q_docs = lax.dynamic_slice_in_dim(doc_ids, first_row, row_count, 0).reshape(row_count, 1)
    k_docs = lax.dynamic_slice_in_dim(pad_docs, first_row, WINDOW + row_count, 0).reshape(1, -1)
    q2 = query_heads.reshape(row_count, -1)
    g2 = grad_out.reshape(row_count, -1)
    k2 = key_heads.reshape(row_count, -1)
    v2 = value_heads.reshape(row_count, -1)
    kv_width = k2.shape[1] // CHUNKS
    bufs = ()
    totals = []
    for c in range(CHUNKS):
        lanes = slice(c * kv_width, (c + 1) * kv_width)
        own = jnp.stack([k2[:, lanes], v2[:, lanes]])
        pieces = forward_exchange(own, is_odd)
        o_buf, dq_buf, *terms = attention(
            q2, g2, pieces, q_docs, k_docs, head_size, c, bufs)
        bufs = (o_buf, dq_buf)
        totals.append(backward_exchange(terms, is_odd))
    attended = o_buf.reshape(query_heads.shape)
    grad_q = dq_buf.reshape(query_heads.shape)
    total = jnp.concatenate(totals, 2)
    grad_k = total[0].astype(jnp.bfloat16).reshape(key_heads.shape)
    grad_v = total[1].astype(jnp.bfloat16).reshape(value_heads.shape)
    return (attended, grad_q, grad_k, grad_v)


def solution(mesh):
    placed = (
        P(("dp", "ctx"), None, None),
        P(("dp", "ctx"), None, None),
        P(("dp", "ctx"), None, None),
        P(("dp", "ctx"), None, None),
        P("dp"),
    )
    return jax.shard_map(
        staged,
        mesh=mesh,
        in_specs=placed,
        out_specs=(
            P(("dp", "ctx"), None, None),
            P(("dp", "ctx"), None, None),
            P(("dp", "ctx"), None, None),
            P(("dp", "ctx"), None, None),
        ),
        check_vma=False,
    )
```
